256 devices in a mesh: asset: 16 (over y, z_hi), earn: 4 (over x), age: 4 (over z_lo, core).
Axes of the slice: x: 4, y: 4, z: 8 (z_hi: 4, z_lo: 2; z = z_hi * 2 + z_lo), core: 2. Of those that a mesh axis runs over, the one named last changes fastest.
Arguments:
- values: float32 [8, 32, 512, 512], P('age', 'earn', 'asset'), may hold values from -6 to 6
- utility: float32 [8, 32, 512, 512], P('age', 'earn', 'asset'), may hold values from -6 to 6
- earn_prob: float32 [5, 32], P(None, 'earn'), may hold values from 0.1 to 1
- support_start: int32 [32], P('earn'), may hold values from 0 to 27, as said below
- liquid_offset: int32 [32, 512], P('earn'), may hold values from 0 to 508
- liquid_weight: float32 [4, 32, 512], P(None, 'earn'), may hold values from 0.05 to 0.45
- illiquid_offset: int32 [32, 512], P('earn'), may hold values from 0 to 508
- illiquid_weight: float32 [4, 32, 512], P(None, 'earn'), may hold values from 0.05 to 0.45
Outputs:
- updated: float32 [8, 32, 512, 512], P('age', 'earn', 'asset')
The draws below stay inside these ranges and needn't reach their ends.
Inputs may be any that keep to these rules, and one draw needn't show every extreme that they name: support_start[e] lies between e - 4 and e, and support_start[e] + 4 is a valid state.
All inputs are finite; a program needn't handle non-finite values.
Results may differ from the reference program's by a relative error of at most 0.00005.
Values sent between devices are 32-bit elements; how exact they have to be, the bound alone decides.
No kernel may reach another device: no remote copies, remote signals or barrier semaphores. Data moves between devices by JAX's collectives and lax.ppermute only.
A program may use at most 64 MiB of HBM per device.

```python
import math
import jax
import jax.numpy as jnp
from jax import lax

A = 512
B = 512
E = 32
REACH = 4
BAND = 4
ITERS = 2
AGES = 8


def draw_support_start(key, part):
    states = jnp.arange(E, dtype=jnp.int32)
    downward = jax.random.randint(key, (E,), 0, REACH + 1).astype(jnp.int32)
    phase = jax.random.randint(jax.random.fold_in(key, 7), (), 0, 4).astype(jnp.int32)
    downward = jnp.where(states % 4 == phase, REACH, downward)
    return jnp.clip(states - downward, 0, E - 1 - REACH).astype(jnp.int32)


def plant(values, own_key, smallest, largest):
    longest = values.shape.index(max(values.shape))
    spots = []
    for shift in (0, 1):
        where = [jax.random.randint(jax.random.fold_in(own_key, axis), (), 0, length) for axis, length in enumerate(values.shape)]
        where[longest] = (where[longest] + shift) % values.shape[longest]
        spots.append(tuple(where))
    return values.at[spots[0]].set(smallest).at[spots[1]].set(largest)


def levels(stream_key, extent, split, least, largest):
    gain = 1.0
    for axis_at, shards_of in split:
        draws = jax.random.uniform(jax.random.fold_in(jax.random.fold_in(stream_key, 6), axis_at), (shards_of,), jnp.float32, least / len(split), largest / len(split))
        gain = gain * jnp.repeat(jnp.exp(draws), extent[axis_at] // shards_of).reshape((-1,) + (1,) * (len(extent) - 1 - axis_at))
    return gain


def normal_values(stream_key, extent, width, limit, cuts=(), kind=jnp.bfloat16):
    level = levels(stream_key, extent, cuts, -0.22, 0.18) if cuts else 1.0
    array = jax.random.normal(stream_key, extent, jnp.float32) * width * level
    return jnp.minimum(jnp.maximum(array, -limit), limit).astype(kind)


def setup_inputs(seed: int = 0) -> dict:
    seeds = jax.random.split(jax.random.key(seed), 9)
    return {
        "values": normal_values(seeds[0], (AGES, E, B, A), 1.0, 6.0, ((0, 4), (1, 4), (2, 16)), jnp.float32),
        "utility": normal_values(seeds[1], (AGES, E, B, A), 1.0, 6.0, ((0, 4), (1, 4), (2, 16)), jnp.float32),
        "earn_prob": jnp.clip(jnp.exp(math.log(1.0) - 2.3025851 * jax.random.uniform(seeds[2], (REACH + 1, E), jnp.float32) ** levels(seeds[2], (REACH + 1, E), ((1, 4),), -0.2, 0.2)), 0.1, 1.0),
        "support_start": draw_support_start(jax.random.fold_in(seeds[8], 71), 0),
        "liquid_offset": plant(jax.random.randint(seeds[4], (E, A), 0, A - BAND + 1), jax.random.fold_in(seeds[4], 1), 0, A - BAND).astype(jnp.int32),
        "liquid_weight": jnp.clip(0.05 + 0.39999999 * jax.random.uniform(seeds[5], (BAND, E, A), jnp.float32) ** levels(seeds[5], (BAND, E, A), ((1, 4),), -0.2, 0.2), 0.05, 0.45),
        "illiquid_offset": plant(jax.random.randint(seeds[6], (E, B), 0, B - BAND + 1), jax.random.fold_in(seeds[6], 1), 0, B - BAND).astype(jnp.int32),
        "illiquid_weight": jnp.clip(0.05 + 0.39999999 * jax.random.uniform(seeds[7], (BAND, E, B), jnp.float32) ** levels(seeds[7], (BAND, E, B), ((1, 4),), -0.2, 0.2), 0.05, 0.45),
    }


DISCOUNT = 0.96


def liquid_one(pieces):
    stacked, offset, weight = pieces
    result = jnp.zeros_like(stacked)
    for number in range(BAND):
        result = result + weight[number][None, None, :] * stacked[:, :, offset + number]
    return result


def illiquid_one(pieces):
    stacked, offset, weight = pieces
    result = jnp.zeros_like(stacked)
    for number in range(BAND):
        result = result + weight[number][None, :, None] * stacked[:, offset + number, :]
    return result


def reference(values, utility, earn_prob, support_start, liquid_offset, liquid_weight, illiquid_offset, illiquid_weight):
    shares = earn_prob / jnp.sum(earn_prob, axis=0, keepdims=True)
    current = values
    for iteration in range(ITERS):
        following = jnp.concatenate([current[1:], jnp.zeros_like(current[:1])], axis=0)
        expected = jnp.zeros_like(current)
        for number in range(REACH + 1):
            expected = expected + shares[number][None, :, None, None] * following[:, support_start + number]
        moved = jnp.moveaxis(expected, 1, 0)
        saved = lax.map(liquid_one, (moved, liquid_offset, jnp.moveaxis(liquid_weight, 1, 0)))
        adjusted = lax.map(illiquid_one, (saved, illiquid_offset, jnp.moveaxis(illiquid_weight, 1, 0)))
        current = utility + DISCOUNT * jnp.moveaxis(adjusted, 0, 1)
    return current
```

```python
import jax
import jax.numpy as jnp
from jax import lax
from jax.sharding import PartitionSpec as P

REACH = 4
BAND = 4
ITERS = 2


DISCOUNT = 0.96
PRECISE = lax.Precision.HIGHEST


def extended(cells, sides, width):
    for axis, dim in sides:
        count = lax.axis_size(axis)
        ends = count - 1
        head = lax.slice_in_dim(cells, 0, width, axis=dim)
        tail = lax.slice_in_dim(cells, cells.shape[dim] - width, cells.shape[dim], axis=dim)
        cells = jnp.concatenate(
            [
                lax.ppermute(tail, axis, [(i, (i + 1) % count) for i in range(ends)]),
                cells,
                lax.ppermute(head, axis, [((i + 1) % count, i) for i in range(ends)]),
            ],
            axis=dim,
        )
    return cells


def passed_along(value, axis, by):
    count = lax.axis_size(axis)
    pairs = [(i, i + by) for i in range(count) if 0 <= i + by < count]
    return lax.ppermute(value, axis, pairs)


def band_matrix(offset, weight):
    extent = offset.shape[1]
    positions = jnp.arange(extent, dtype=jnp.int32)
    matrix = jnp.zeros((offset.shape[0], extent, extent), jnp.float32)
    for number in range(BAND):
        matrix = matrix + jnp.where(
            positions[None, :, None] == (offset + number)[:, None, :],
            weight[number][:, None, :],
            0.0,
        )
    return matrix


def expectation(stacked, earn_prob, support_start):
    padded = extended(stacked, (("earn", 1),), REACH)
    states_here = stacked.shape[1]
    first_state = lax.axis_index("earn") * states_here
    slots = jnp.arange(states_here + 2 * REACH, dtype=jnp.int32)
    prob_sum = jnp.sum(earn_prob, axis=0)
    mixing = jnp.zeros((states_here, states_here + 2 * REACH), jnp.float32)
    for number in range(REACH + 1):
        target = support_start + number - first_state + REACH
        mixing = mixing + jnp.where(
            slots[None, :] == target[:, None], (earn_prob[number] / prob_sum)[:, None], 0.0
        )
    return jnp.einsum("ij,tjxy->tixy", mixing, padded, precision=PRECISE)


def continuation(current, earn_prob, support_start):
    arrived = passed_along(current[:1], "age", -1)
    return expectation(jnp.concatenate([current[1:], arrived], axis=0), earn_prob, support_start)


def along_lanes(stacked, matrix):
    return jnp.einsum("terc,ecn->tern", stacked, matrix, precision=PRECISE)


def flipped(stacked):
    ages, states, rows, lanes = stacked.shape
    count = lax.axis_size("asset")
    piece = lanes // count
    flat = stacked.reshape(ages * states * rows, lanes).T.reshape(count, piece, ages * states * rows)
    got = lax.all_to_all(flat, "asset", 0, 0, tiled=True)
    got = got.reshape(count, piece, ages, states, rows)
    return jnp.transpose(got, (2, 3, 1, 0, 4)).reshape(ages, states, piece, count * rows)


def local(
    values,
    utility,
    earn_prob,
    support_start,
    liquid_offset,
    liquid_weight,
    illiquid_offset,
    illiquid_weight,
):
    liquid_map = band_matrix(liquid_offset, liquid_weight)
    illiquid_map = band_matrix(illiquid_offset, illiquid_weight)

    expected = continuation(values, earn_prob, support_start)
    saved = along_lanes(expected, liquid_map)
    adjusted = along_lanes(flipped(saved), illiquid_map)
    current = flipped(utility) + DISCOUNT * adjusted

    expected = continuation(current, earn_prob, support_start)
    moved = along_lanes(expected, illiquid_map)
    adjusted = along_lanes(flipped(moved), liquid_map)
    return utility + DISCOUNT * adjusted


def solution(mesh):
    return jax.shard_map(
        local,
        mesh=mesh,
        in_specs=(
            P("age", "earn", "asset", None),
            P("age", "earn", "asset", None),
            P(None, "earn"),
            P("earn"),
            P("earn", None),
            P(None, "earn", None),
            P("earn", None),
            P(None, "earn", None),
        ),
        out_specs=P("age", "earn", "asset", None),
        check_vma=False,
    )
```

```python
import jax
import jax.numpy as jnp
from jax import lax
from jax.sharding import PartitionSpec as P

REACH = 4
BAND = 4
ITERS = 2


DISCOUNT = 0.96
PRECISE = lax.Precision.HIGHEST


def extended(cells, sides, width):
    for axis, dim in sides:
        count = lax.axis_size(axis)
        ends = count - 1
        head = lax.slice_in_dim(cells, 0, width, axis=dim)
        tail = lax.slice_in_dim(cells, cells.shape[dim] - width, cells.shape[dim], axis=dim)
        cells = jnp.concatenate(
            [
                lax.ppermute(tail, axis, [(i, (i + 1) % count) for i in range(ends)]),
                cells,
                lax.ppermute(head, axis, [((i + 1) % count, i) for i in range(ends)]),
            ],
            axis=dim,
        )
    return cells


def passed_along(value, axis, by):
    count = lax.axis_size(axis)
    pairs = [(i, i + by) for i in range(count) if 0 <= i + by < count]
    return lax.ppermute(value, axis, pairs)


def band_matrix(offset, weight):
    extent = offset.shape[1]
    positions = jnp.arange(extent, dtype=jnp.int32)
    matrix = jnp.zeros((offset.shape[0], extent, extent), jnp.float32)
    for number in range(BAND):
        matrix = matrix + jnp.where(
            positions[None, :, None] == (offset + number)[:, None, :],
            weight[number][:, None, :],
            0.0,
        )
    return matrix


def expectation(stacked, earn_prob, support_start):
    padded = extended(stacked, (("earn", 1),), REACH)
    states_here = stacked.shape[1]
    first_state = lax.axis_index("earn") * states_here
    slots = jnp.arange(states_here + 2 * REACH, dtype=jnp.int32)
    prob_sum = jnp.sum(earn_prob, axis=0)
    mixing = jnp.zeros((states_here, states_here + 2 * REACH), jnp.float32)
    for number in range(REACH + 1):
        target = support_start + number - first_state + REACH
        mixing = mixing + jnp.where(
            slots[None, :] == target[:, None], (earn_prob[number] / prob_sum)[:, None], 0.0
        )
    return jnp.einsum("ij,tjxy->tixy", mixing, padded, precision=PRECISE)


def continuation(current, earn_prob, support_start):
    arrived = passed_along(current[:1], "age", -1)
    return expectation(jnp.concatenate([current[1:], arrived], axis=0), earn_prob, support_start)


def along_lanes(stacked, matrix):
    return jnp.einsum("terc,ecn->tern", stacked, matrix, precision=lax.Precision.HIGH)


def flipped(stacked):
    ages, states, rows, lanes = stacked.shape
    count = lax.axis_size("asset")
    piece = lanes // count
    flat = stacked.reshape(ages * states * rows, lanes).T.reshape(count, piece, ages * states * rows)
    got = lax.all_to_all(flat, "asset", 0, 0, tiled=True)
    got = got.reshape(count, piece, ages, states, rows)
    return jnp.transpose(got, (2, 3, 1, 0, 4)).reshape(ages, states, piece, count * rows)


def local(
    values,
    utility,
    earn_prob,
    support_start,
    liquid_offset,
    liquid_weight,
    illiquid_offset,
    illiquid_weight,
):
    liquid_map = band_matrix(liquid_offset, liquid_weight)
    illiquid_map = band_matrix(illiquid_offset, illiquid_weight)

    expected = continuation(values, earn_prob, support_start)
    saved = along_lanes(expected, liquid_map)
    adjusted = along_lanes(flipped(saved), illiquid_map)
    current = flipped(utility) + DISCOUNT * adjusted

    expected = continuation(current, earn_prob, support_start)
    moved = along_lanes(expected, illiquid_map)
    adjusted = along_lanes(flipped(moved), liquid_map)
    return utility + DISCOUNT * adjusted


def solution(mesh):
    return jax.shard_map(
        local,
        mesh=mesh,
        in_specs=(
            P("age", "earn", "asset", None),
            P("age", "earn", "asset", None),
            P(None, "earn"),
            P("earn"),
            P("earn", None),
            P(None, "earn", None),
            P("earn", None),
            P(None, "earn", None),
        ),
        out_specs=P("age", "earn", "asset", None),
        check_vma=False,
    )
```

```python
import jax
import jax.numpy as jnp
from jax import lax
from jax.experimental import pallas as pl
from jax.experimental.pallas import tpu as pltpu
from jax.sharding import PartitionSpec as P

REACH = 4
BAND = 4
ITERS = 2


DISCOUNT = 0.96
PRECISE = lax.Precision.HIGHEST


def extended(cells, sides, width):
    for axis, dim in sides:
        count = lax.axis_size(axis)
        ends = count - 1
        head = lax.slice_in_dim(cells, 0, width, axis=dim)
        tail = lax.slice_in_dim(cells, cells.shape[dim] - width, cells.shape[dim], axis=dim)
        cells = jnp.concatenate(
            [
                lax.ppermute(tail, axis, [(i, (i + 1) % count) for i in range(ends)]),
                cells,
                lax.ppermute(head, axis, [((i + 1) % count, i) for i in range(ends)]),
            ],
            axis=dim,
        )
    return cells


def passed_along(value, axis, by):
    count = lax.axis_size(axis)
    pairs = [(i, i + by) for i in range(count) if 0 <= i + by < count]
    return lax.ppermute(value, axis, pairs)


def band_matrix(offset, weight):
    extent = offset.shape[1]
    positions = jnp.arange(extent, dtype=jnp.int32)
    matrix = jnp.zeros((offset.shape[0], extent, extent), jnp.float32)
    for number in range(BAND):
        matrix = matrix + jnp.where(
            positions[None, :, None] == (offset + number)[:, None, :],
            weight[number][:, None, :],
            0.0,
        )
    return matrix


def expectation(stacked, earn_prob, support_start):
    padded = extended(stacked, (("earn", 1),), REACH)
    states_here = stacked.shape[1]
    first_state = lax.axis_index("earn") * states_here
    slots = jnp.arange(states_here + 2 * REACH, dtype=jnp.int32)
    prob_sum = jnp.sum(earn_prob, axis=0)
    mixing = jnp.zeros((states_here, states_here + 2 * REACH), jnp.float32)
    for number in range(REACH + 1):
        target = support_start + number - first_state + REACH
        mixing = mixing + jnp.where(
            slots[None, :] == target[:, None], (earn_prob[number] / prob_sum)[:, None], 0.0
        )
    return jnp.einsum("ij,tjxy->tixy", mixing, padded, precision=PRECISE)


def continuation(current, earn_prob, support_start):
    arrived = passed_along(current[:1], "age", -1)
    return expectation(jnp.concatenate([current[1:], arrived], axis=0), earn_prob, support_start)


def along_lanes(stacked, matrix):
    return jnp.einsum("terc,ecn->tern", stacked, matrix, precision=lax.Precision.HIGH)


def _gather_kernel(src_ref, dst_ref):
    count, piece, lanes = src_ref.shape
    slabs = dst_ref.shape[0]
    width = lanes // slabs
    lane = lax.broadcasted_iota(jnp.int32, (piece, lanes), 1)
    for w in range(count // slabs):
        outs = [None] * slabs
        for u in range(slabs):
            x = src_ref[w * slabs + u]
            keep = (lane >= u * width) & (lane < (u + 1) * width)
            for s in range(slabs):
                shift = ((u - s) * width) % lanes
                y = pltpu.roll(x, shift, 1) if shift else x
                outs[s] = y if u == 0 else jnp.where(keep, y, outs[s])
        for s in range(slabs):
            dst_ref[s, :, pl.ds(w * lanes, lanes)] = outs[s]


def regroup(got):
    count, piece, lanes = got.shape
    width = lanes // count
    slabs = 128 // width
    nbytes = got.size * got.dtype.itemsize
    return pl.pallas_call(
        _gather_kernel,
        grid=(lanes // 128,),
        in_specs=[pl.BlockSpec((count, piece, 128), lambda k: (0, 0, k))],
        out_specs=pl.BlockSpec((slabs, piece, count * width), lambda k: (k, 0, 0)),
        out_shape=jax.ShapeDtypeStruct((lanes // width, piece, count * width), got.dtype),
        cost_estimate=pl.CostEstimate(flops=0, transcendentals=0, bytes_accessed=2 * nbytes),
    )(got)


def flipped(stacked):
    ages, states, rows, lanes = stacked.shape
    count = lax.axis_size("asset")
    piece = lanes // count
    flat = stacked.reshape(ages * states * rows, lanes).T.reshape(count, piece, ages * states * rows)
    got = lax.all_to_all(flat, "asset", 0, 0, tiled=True)
    return regroup(got).reshape(ages, states, piece, count * rows)


def local(
    values,
    utility,
    earn_prob,
    support_start,
    liquid_offset,
    liquid_weight,
    illiquid_offset,
    illiquid_weight,
):
    liquid_map = band_matrix(liquid_offset, liquid_weight)
    illiquid_map = band_matrix(illiquid_offset, illiquid_weight)

    expected = continuation(values, earn_prob, support_start)
    saved = along_lanes(expected, liquid_map)
    adjusted = along_lanes(flipped(saved), illiquid_map)
    current = flipped(utility) + DISCOUNT * adjusted

    expected = continuation(current, earn_prob, support_start)
    moved = along_lanes(expected, illiquid_map)
    adjusted = along_lanes(flipped(moved), liquid_map)
    return utility + DISCOUNT * adjusted


def solution(mesh):
    return jax.shard_map(
        local,
        mesh=mesh,
        in_specs=(
            P("age", "earn", "asset", None),
            P("age", "earn", "asset", None),
            P(None, "earn"),
            P("earn"),
            P("earn", None),
            P(None, "earn", None),
            P("earn", None),
            P(None, "earn", None),
        ),
        out_specs=P("age", "earn", "asset", None),
        check_vma=False,
    )
```

```python
import jax
import jax.numpy as jnp
from jax import lax
from jax.experimental import pallas as pl
from jax.experimental.pallas import tpu as pltpu
from jax.sharding import PartitionSpec as P

REACH = 4
BAND = 4
ITERS = 2


DISCOUNT = 0.96
PRECISE = lax.Precision.HIGHEST


def extended(cells, sides, width):
    for axis, dim in sides:
        count = lax.axis_size(axis)
        ends = count - 1
        head = lax.slice_in_dim(cells, 0, width, axis=dim)
        tail = lax.slice_in_dim(cells, cells.shape[dim] - width, cells.shape[dim], axis=dim)
        cells = jnp.concatenate(
            [
                lax.ppermute(tail, axis, [(i, (i + 1) % count) for i in range(ends)]),
                cells,
                lax.ppermute(head, axis, [((i + 1) % count, i) for i in range(ends)]),
            ],
            axis=dim,
        )
    return cells


def passed_along(value, axis, by):
    count = lax.axis_size(axis)
    pairs = [(i, i + by) for i in range(count) if 0 <= i + by < count]
    return lax.ppermute(value, axis, pairs)


def band_matrix(offset, weight):
    extent = offset.shape[1]
    positions = jnp.arange(extent, dtype=jnp.int32)
    matrix = jnp.zeros((offset.shape[0], extent, extent), jnp.float32)
    for number in range(BAND):
        matrix = matrix + jnp.where(
            positions[None, :, None] == (offset + number)[:, None, :],
            weight[number][:, None, :],
            0.0,
        )
    return matrix


def expectation(stacked, earn_prob, support_start):
    padded = extended(stacked, (("earn", 1),), REACH)
    states_here = stacked.shape[1]
    first_state = lax.axis_index("earn") * states_here
    slots = jnp.arange(states_here + 2 * REACH, dtype=jnp.int32)
    prob_sum = jnp.sum(earn_prob, axis=0)
    mixing = jnp.zeros((states_here, states_here + 2 * REACH), jnp.float32)
    for number in range(REACH + 1):
        target = support_start + number - first_state + REACH
        mixing = mixing + jnp.where(
            slots[None, :] == target[:, None], (earn_prob[number] / prob_sum)[:, None], 0.0
        )
    return jnp.einsum("ij,tjxy->tixy", mixing, padded, precision=PRECISE)


def continuation(current, earn_prob, support_start):
    arrived = passed_along(current[:1], "age", -1)
    return expectation(jnp.concatenate([current[1:], arrived], axis=0), earn_prob, support_start)


def along_lanes(stacked, matrix):
    return jnp.einsum("terc,ecn->tern", stacked, matrix, precision=lax.Precision.HIGH)


def _gather_kernel(src_ref, dst_ref):
    count, piece, lanes = src_ref.shape
    slabs = dst_ref.shape[0]
    width = lanes // slabs
    lane = lax.broadcasted_iota(jnp.int32, (piece, lanes), 1)
    for w in range(count // slabs):
        outs = [None] * slabs
        for u in range(slabs):
            x = src_ref[w * slabs + u]
            keep = (lane >= u * width) & (lane < (u + 1) * width)
            for s in range(slabs):
                shift = ((u - s) * width) % lanes
                y = pltpu.roll(x, shift, 1) if shift else x
                outs[s] = y if u == 0 else jnp.where(keep, y, outs[s])
        for s in range(slabs):
            dst_ref[s, :, pl.ds(w * lanes, lanes)] = outs[s]


def regroup(got):
    count, piece, lanes = got.shape
    width = lanes // count
    slabs = 128 // width
    nbytes = got.size * got.dtype.itemsize
    return pl.pallas_call(
        _gather_kernel,
        grid=(lanes // 128,),
        in_specs=[pl.BlockSpec((count, piece, 128), lambda k: (0, 0, k))],
        out_specs=pl.BlockSpec((slabs, piece, count * width), lambda k: (k, 0, 0)),
        out_shape=jax.ShapeDtypeStruct((lanes // width, piece, count * width), got.dtype),
        cost_estimate=pl.CostEstimate(flops=0, transcendentals=0, bytes_accessed=2 * nbytes),
    )(got)


def flipped(stacked):
    ages, states, rows, lanes = stacked.shape
    count = lax.axis_size("asset")
    piece = lanes // count
    flat = stacked.reshape(ages * states * rows, lanes).T.reshape(count, piece, ages * states * rows)
    got = lax.all_to_all(flat, "asset", 0, 0, tiled=True)
    return regroup(got).reshape(ages, states, piece, count * rows)


def local(
    values,
    utility,
    earn_prob,
    support_start,
    liquid_offset,
    liquid_weight,
    illiquid_offset,
    illiquid_weight,
):
    liquid_map = band_matrix(liquid_offset, liquid_weight)
    illiquid_map = band_matrix(illiquid_offset, illiquid_weight)
    liquid_map, illiquid_map = lax.optimization_barrier((liquid_map, illiquid_map))

    expected = continuation(values, earn_prob, support_start)
    saved = along_lanes(expected, liquid_map)
    adjusted = along_lanes(flipped(saved), illiquid_map)
    current = flipped(utility) + DISCOUNT * adjusted

    expected = continuation(current, earn_prob, support_start)
    moved = along_lanes(expected, illiquid_map)
    adjusted = along_lanes(flipped(moved), liquid_map)
    return utility + DISCOUNT * adjusted


def solution(mesh):
    return jax.shard_map(
        local,
        mesh=mesh,
        in_specs=(
            P("age", "earn", "asset", None),
            P("age", "earn", "asset", None),
            P(None, "earn"),
            P("earn"),
            P("earn", None),
            P(None, "earn", None),
            P("earn", None),
            P(None, "earn", None),
        ),
        out_specs=P("age", "earn", "asset", None),
        check_vma=False,
    )
```

```python
import jax
import jax.numpy as jnp
from jax import lax
from jax.experimental import pallas as pl
from jax.experimental.pallas import tpu as pltpu
from jax.sharding import PartitionSpec as P

REACH = 4
BAND = 4
ITERS = 2


DISCOUNT = 0.96
PRECISE = lax.Precision.HIGHEST


def band_matrix(offset, weight):
    extent = offset.shape[1]
    positions = jnp.arange(extent, dtype=jnp.int32)
    matrix = jnp.zeros((offset.shape[0], extent, extent), jnp.float32)
    for number in range(BAND):
        matrix = matrix + jnp.where(
            positions[None, :, None] == (offset + number)[:, None, :],
            weight[number][:, None, :],
            0.0,
        )
    return matrix


def neighbours(current):
    states = current.shape[1]
    ages = lax.axis_size("age")
    earns = lax.axis_size("earn")
    axes = ("earn", "age")

    def moved(value, by_earn, by_age):
        pairs = []
        for e in range(earns):
            for a in range(ages):
                te, ta = e + by_earn, a + by_age
                if 0 <= te < earns and 0 <= ta < ages:
                    pairs.append((e * ages + a, te * ages + ta))
        return lax.ppermute(value, axes, pairs)

    head = slice(0, REACH)
    tail = slice(states - REACH, states)
    here = jnp.concatenate(
        [moved(current[1:, tail], 1, 0), current[1:], moved(current[1:, head], -1, 0)], axis=1
    )
    above = jnp.concatenate(
        [moved(current[:1, tail], 1, -1), moved(current[:1], 0, -1), moved(current[:1, head], -1, -1)],
        axis=1,
    )
    return jnp.concatenate([here, above], axis=0)


def continuation(current, earn_prob, support_start):
    padded = neighbours(current)
    states_here = current.shape[1]
    first_state = lax.axis_index("earn") * states_here
    slots = jnp.arange(states_here + 2 * REACH, dtype=jnp.int32)
    prob_sum = jnp.sum(earn_prob, axis=0)
    mixing = jnp.zeros((states_here, states_here + 2 * REACH), jnp.float32)
    for number in range(REACH + 1):
        target = support_start + number - first_state + REACH
        mixing = mixing + jnp.where(
            slots[None, :] == target[:, None], (earn_prob[number] / prob_sum)[:, None], 0.0
        )
    return jnp.einsum("ij,tjxy->tixy", mixing, padded, precision=PRECISE)


def along_lanes(stacked, matrix):
    return jnp.einsum("terc,ecn->tern", stacked, matrix, precision=lax.Precision.HIGH)


def _gather_kernel(src_ref, dst_ref):
    count, piece, lanes = src_ref.shape
    slabs = dst_ref.shape[0]
    width = lanes // slabs
    lane = lax.broadcasted_iota(jnp.int32, (piece, lanes), 1)
    for w in range(count // slabs):
        outs = [None] * slabs
        for u in range(slabs):
            x = src_ref[w * slabs + u]
            keep = (lane >= u * width) & (lane < (u + 1) * width)
            for s in range(slabs):
                shift = ((u - s) * width) % lanes
                y = pltpu.roll(x, shift, 1) if shift else x
                outs[s] = y if u == 0 else jnp.where(keep, y, outs[s])
        for s in range(slabs):
            dst_ref[s, :, pl.ds(w * lanes, lanes)] = outs[s]


def regroup(got):
    count, piece, lanes = got.shape
    width = lanes // count
    slabs = 128 // width
    nbytes = got.size * got.dtype.itemsize
    return pl.pallas_call(
        _gather_kernel,
        grid=(lanes // 128,),
        in_specs=[pl.BlockSpec((count, piece, 128), lambda k: (0, 0, k))],
        out_specs=pl.BlockSpec((slabs, piece, count * width), lambda k: (k, 0, 0)),
        out_shape=jax.ShapeDtypeStruct((lanes // width, piece, count * width), got.dtype),
        cost_estimate=pl.CostEstimate(flops=0, transcendentals=0, bytes_accessed=2 * nbytes),
    )(got)


def flipped(stacked):
    ages, states, rows, lanes = stacked.shape
    count = lax.axis_size("asset")
    piece = lanes // count
    flat = stacked.reshape(ages * states * rows, lanes).T.reshape(count, piece, ages * states * rows)
    got = lax.all_to_all(flat, "asset", 0, 0, tiled=True)
    return regroup(got).reshape(ages, states, piece, count * rows)


def local(
    values,
    utility,
    earn_prob,
    support_start,
    liquid_offset,
    liquid_weight,
    illiquid_offset,
    illiquid_weight,
):
    liquid_map = band_matrix(liquid_offset, liquid_weight)
    illiquid_map = band_matrix(illiquid_offset, illiquid_weight)

    expected = continuation(values, earn_prob, support_start)
    saved = along_lanes(expected, liquid_map)
    adjusted = along_lanes(flipped(saved), illiquid_map)
    current = flipped(utility) + DISCOUNT * adjusted

    expected = continuation(current, earn_prob, support_start)
    moved = along_lanes(expected, illiquid_map)
    adjusted = along_lanes(flipped(moved), liquid_map)
    return utility + DISCOUNT * adjusted


def solution(mesh):
    return jax.shard_map(
        local,
        mesh=mesh,
        in_specs=(
            P("age", "earn", "asset", None),
            P("age", "earn", "asset", None),
            P(None, "earn"),
            P("earn"),
            P("earn", None),
            P(None, "earn", None),
            P("earn", None),
            P(None, "earn", None),
        ),
        out_specs=P("age", "earn", "asset", None),
        check_vma=False,
    )
```

```python
import jax
import jax.numpy as jnp
from jax import lax
from jax.experimental import pallas as pl
from jax.experimental.pallas import tpu as pltpu
from jax.sharding import PartitionSpec as P

REACH = 4
BAND = 4
ITERS = 2


DISCOUNT = 0.96
PRECISE = lax.Precision.HIGHEST


def band_matrix(offset, weight):
    extent = offset.shape[1]
    positions = jnp.arange(extent, dtype=jnp.int32)
    matrix = jnp.zeros((offset.shape[0], extent, extent), jnp.float32)
    for number in range(BAND):
        matrix = matrix + jnp.where(
            positions[None, :, None] == (offset + number)[:, None, :],
            weight[number][:, None, :],
            0.0,
        )
    return matrix


def neighbours(current):
    states = current.shape[1]
    ages = lax.axis_size("age")
    earns = lax.axis_size("earn")
    axes = ("earn", "age")

    def moved(value, by_earn, by_age):
        pairs = []
        for e in range(earns):
            for a in range(ages):
                te, ta = e + by_earn, a + by_age
                if 0 <= te < earns and 0 <= ta < ages:
                    pairs.append((e * ages + a, te * ages + ta))
        return lax.ppermute(value, axes, pairs)

    head = slice(0, REACH)
    tail = slice(states - REACH, states)
    here = jnp.concatenate(
        [moved(current[1:, tail], 1, 0), current[1:], moved(current[1:, head], -1, 0)], axis=1
    )
    above = jnp.concatenate(
        [moved(current[:1, tail], 1, -1), moved(current[:1], 0, -1), moved(current[:1, head], -1, -1)],
        axis=1,
    )
    return jnp.concatenate([here, above], axis=0)


def continuation(current, earn_prob, support_start):
    padded = neighbours(current)
    states_here = current.shape[1]
    first_state = lax.axis_index("earn") * states_here
    slots = jnp.arange(states_here + 2 * REACH, dtype=jnp.int32)
    prob_sum = jnp.sum(earn_prob, axis=0)
    mixing = jnp.zeros((states_here, states_here + 2 * REACH), jnp.float32)
    for number in range(REACH + 1):
        target = support_start + number - first_state + REACH
        mixing = mixing + jnp.where(
            slots[None, :] == target[:, None], (earn_prob[number] / prob_sum)[:, None], 0.0
        )
    return jnp.einsum("ij,tjxy->tixy", mixing, padded, precision=PRECISE)


def along_lanes(stacked, matrix):
    return jnp.einsum("terc,ecn->tern", stacked, matrix, precision=lax.Precision.HIGH)


def _gather_kernel(src_ref, dst_ref):
    count, piece, lanes = src_ref.shape
    width = dst_ref.shape[2] // count
    slabs = 128 // width
    lane = lax.broadcasted_iota(jnp.int32, (piece, 128), 1)
    for k in range(lanes // 128):
        for w in range(count // slabs):
            outs = [None] * slabs
            for u in range(slabs):
                x = src_ref[w * slabs + u, :, pl.ds(k * 128, 128)]
                keep = (lane >= u * width) & (lane < (u + 1) * width)
                for s in range(slabs):
                    shift = ((u - s) * width) % 128
                    y = pltpu.roll(x, shift, 1) if shift else x
                    outs[s] = y if u == 0 else jnp.where(keep, y, outs[s])
            for s in range(slabs):
                dst_ref[k * slabs + s, :, pl.ds(w * 128, 128)] = outs[s]


def regroup(got):
    count, piece, lanes = got.shape
    width = lanes // count
    nbytes = got.size * got.dtype.itemsize
    return pl.pallas_call(
        _gather_kernel,
        in_specs=[pl.BlockSpec(memory_space=pltpu.VMEM)],
        out_specs=pl.BlockSpec(memory_space=pltpu.VMEM),
        out_shape=jax.ShapeDtypeStruct((lanes // width, piece, count * width), got.dtype),
        cost_estimate=pl.CostEstimate(flops=0, transcendentals=0, bytes_accessed=2 * nbytes),
    )(got)


def flipped(stacked):
    ages, states, rows, lanes = stacked.shape
    count = lax.axis_size("asset")
    piece = lanes // count
    flat = stacked.reshape(ages * states * rows, lanes).T.reshape(count, piece, ages * states * rows)
    got = lax.all_to_all(flat, "asset", 0, 0, tiled=True)
    return regroup(got).reshape(ages, states, piece, count * rows)


def local(
    values,
    utility,
    earn_prob,
    support_start,
    liquid_offset,
    liquid_weight,
    illiquid_offset,
    illiquid_weight,
):
    liquid_map = band_matrix(liquid_offset, liquid_weight)
    illiquid_map = band_matrix(illiquid_offset, illiquid_weight)

    expected = continuation(values, earn_prob, support_start)
    saved = along_lanes(expected, liquid_map)
    adjusted = along_lanes(flipped(saved), illiquid_map)
    current = flipped(utility) + DISCOUNT * adjusted

    expected = continuation(current, earn_prob, support_start)
    moved = along_lanes(expected, illiquid_map)
    adjusted = along_lanes(flipped(moved), liquid_map)
    return utility + DISCOUNT * adjusted


def solution(mesh):
    return jax.shard_map(
        local,
        mesh=mesh,
        in_specs=(
            P("age", "earn", "asset", None),
            P("age", "earn", "asset", None),
            P(None, "earn"),
            P("earn"),
            P("earn", None),
            P(None, "earn", None),
            P("earn", None),
            P(None, "earn", None),
        ),
        out_specs=P("age", "earn", "asset", None),
        check_vma=False,
    )
```

```python
import jax
import jax.numpy as jnp
from jax import lax
from jax.experimental import pallas as pl
from jax.experimental.pallas import tpu as pltpu
from jax.sharding import PartitionSpec as P

REACH = 4
BAND = 4
ITERS = 2


DISCOUNT = 0.96
PRECISE = lax.Precision.HIGHEST


def band_matrix(offset, weight):
    extent = offset.shape[1]
    positions = jnp.arange(extent, dtype=jnp.int32)
    matrix = jnp.zeros((offset.shape[0], extent, extent), jnp.float32)
    for number in range(BAND):
        matrix = matrix + jnp.where(
            positions[None, :, None] == (offset + number)[:, None, :],
            weight[number][:, None, :],
            0.0,
        )
    return matrix


def neighbours(current):
    states = current.shape[1]
    ages = lax.axis_size("age")
    earns = lax.axis_size("earn")
    axes = ("earn", "age")

    def moved(value, by_earn, by_age):
        pairs = []
        for e in range(earns):
            for a in range(ages):
                te, ta = e + by_earn, a + by_age
                if 0 <= te < earns and 0 <= ta < ages:
                    pairs.append((e * ages + a, te * ages + ta))
        return lax.ppermute(value, axes, pairs)

    head = slice(0, REACH)
    tail = slice(states - REACH, states)
    here = jnp.concatenate(
        [moved(current[1:, tail], 1, 0), current[1:], moved(current[1:, head], -1, 0)], axis=1
    )
    above = jnp.concatenate(
        [moved(current[:1, tail], 1, -1), moved(current[:1], 0, -1), moved(current[:1, head], -1, -1)],
        axis=1,
    )
    return jnp.concatenate([here, above], axis=0)


def continuation(current, earn_prob, support_start):
    padded = neighbours(current)
    states_here = current.shape[1]
    first_state = lax.axis_index("earn") * states_here
    slots = jnp.arange(states_here + 2 * REACH, dtype=jnp.int32)
    prob_sum = jnp.sum(earn_prob, axis=0)
    mixing = jnp.zeros((states_here, states_here + 2 * REACH), jnp.float32)
    for number in range(REACH + 1):
        target = support_start + number - first_state + REACH
        mixing = mixing + jnp.where(
            slots[None, :] == target[:, None], (earn_prob[number] / prob_sum)[:, None], 0.0
        )
    return jnp.einsum("ij,tjxy->tixy", mixing, padded, precision=PRECISE)


def along_lanes(stacked, matrix):
    return jnp.einsum("terc,ecn->tern", stacked, matrix, precision=lax.Precision.HIGH)


def _gather_kernel(src_ref, dst_ref):
    count, piece, lanes = src_ref.shape
    width = dst_ref.shape[2] // count
    slabs = 128 // width
    lane = lax.broadcasted_iota(jnp.int32, (piece, 128), 1)
    for k in range(lanes // 128):
        for w in range(count // slabs):
            outs = [None] * slabs
            for u in range(slabs):
                x = src_ref[w * slabs + u, :, pl.ds(k * 128, 128)]
                keep = (lane >= u * width) & (lane < (u + 1) * width)
                for s in range(slabs):
                    shift = ((u - s) * width) % 128
                    y = pltpu.roll(x, shift, 1) if shift else x
                    outs[s] = y if u == 0 else jnp.where(keep, y, outs[s])
            for s in range(slabs):
                dst_ref[k * slabs + s, :, pl.ds(w * 128, 128)] = outs[s]


def regroup(got):
    count, piece, lanes = got.shape
    width = lanes // count
    nbytes = got.size * got.dtype.itemsize
    return pl.pallas_call(
        _gather_kernel,
        in_specs=[pl.BlockSpec(memory_space=pltpu.VMEM)],
        out_specs=pl.BlockSpec(memory_space=pltpu.VMEM),
        out_shape=jax.ShapeDtypeStruct((lanes // width, piece, count * width), got.dtype),
        cost_estimate=pl.CostEstimate(flops=0, transcendentals=0, bytes_accessed=2 * nbytes),
    )(got)


def flipped(stacked):
    ages, states, rows, lanes = stacked.shape
    count = lax.axis_size("asset")
    piece = lanes // count
    flat = stacked.reshape(ages * states * rows, lanes).T.reshape(count, piece, ages * states * rows)
    got = lax.all_to_all(flat, "asset", 0, 0, tiled=True)
    return regroup(got).reshape(ages, states, piece, count * rows)


def local(
    values,
    utility,
    earn_prob,
    support_start,
    liquid_offset,
    liquid_weight,
    illiquid_offset,
    illiquid_weight,
):
    liquid_map = band_matrix(liquid_offset, liquid_weight)
    illiquid_map = band_matrix(illiquid_offset, illiquid_weight)

    expected = continuation(values, earn_prob, support_start)
    saved = along_lanes(expected, liquid_map)
    adjusted = along_lanes(flipped(saved), illiquid_map)

    carried = flipped(continuation(utility, earn_prob, support_start))
    expected = carried + DISCOUNT * continuation(adjusted, earn_prob, support_start)
    moved = along_lanes(expected, illiquid_map)
    adjusted = along_lanes(flipped(moved), liquid_map)
    return utility + DISCOUNT * adjusted


def solution(mesh):
    return jax.shard_map(
        local,
        mesh=mesh,
        in_specs=(
            P("age", "earn", "asset", None),
            P("age", "earn", "asset", None),
            P(None, "earn"),
            P("earn"),
            P("earn", None),
            P(None, "earn", None),
            P("earn", None),
            P(None, "earn", None),
        ),
        out_specs=P("age", "earn", "asset", None),
        check_vma=False,
    )
```

```python
import jax
import jax.numpy as jnp
from jax import lax
from jax.experimental import pallas as pl
from jax.experimental.pallas import tpu as pltpu
from jax.sharding import PartitionSpec as P

REACH = 4
BAND = 4
ITERS = 2


DISCOUNT = 0.96
PRECISE = lax.Precision.HIGHEST


def band_matrix(offset, weight):
    extent = offset.shape[1]
    positions = jnp.arange(extent, dtype=jnp.int32)
    matrix = jnp.zeros((offset.shape[0], extent, extent), jnp.float32)
    for number in range(BAND):
        matrix = matrix + jnp.where(
            positions[None, :, None] == (offset + number)[:, None, :],
            weight[number][:, None, :],
            0.0,
        )
    return matrix


def neighbours(current):
    states = current.shape[1]
    ages = lax.axis_size("age")
    earns = lax.axis_size("earn")
    axes = ("earn", "age")

    def moved(value, by_earn, by_age):
        pairs = []
        for e in range(earns):
            for a in range(ages):
                te, ta = e + by_earn, a + by_age
                if 0 <= te < earns and 0 <= ta < ages:
                    pairs.append((e * ages + a, te * ages + ta))
        return lax.ppermute(value, axes, pairs)

    head = slice(0, REACH)
    tail = slice(states - REACH, states)
    here = jnp.concatenate(
        [moved(current[1:, tail], 1, 0), current[1:], moved(current[1:, head], -1, 0)], axis=1
    )
    above = jnp.concatenate(
        [moved(current[:1, tail], 1, -1), moved(current[:1], 0, -1), moved(current[:1, head], -1, -1)],
        axis=1,
    )
    return jnp.concatenate([here, above], axis=0)


def continuation(current, earn_prob, support_start):
    padded = neighbours(current)
    states_here = current.shape[1]
    first_state = lax.axis_index("earn") * states_here
    slots = jnp.arange(states_here + 2 * REACH, dtype=jnp.int32)
    prob_sum = jnp.sum(earn_prob, axis=0)
    mixing = jnp.zeros((states_here, states_here + 2 * REACH), jnp.float32)
    for number in range(REACH + 1):
        target = support_start + number - first_state + REACH
        mixing = mixing + jnp.where(
            slots[None, :] == target[:, None], (earn_prob[number] / prob_sum)[:, None], 0.0
        )
    return jnp.einsum("ij,tjxy->tixy", mixing, padded, precision=lax.Precision.HIGH)


def along_lanes(stacked, matrix):
    return jnp.einsum("terc,ecn->tern", stacked, matrix, precision=lax.Precision.HIGH)


def _gather_kernel(src_ref, dst_ref):
    count, piece, lanes = src_ref.shape
    width = dst_ref.shape[2] // count
    slabs = 128 // width
    lane = lax.broadcasted_iota(jnp.int32, (piece, 128), 1)
    for k in range(lanes // 128):
        for w in range(count // slabs):
            outs = [None] * slabs
            for u in range(slabs):
                x = src_ref[w * slabs + u, :, pl.ds(k * 128, 128)]
                keep = (lane >= u * width) & (lane < (u + 1) * width)
                for s in range(slabs):
                    shift = ((u - s) * width) % 128
                    y = pltpu.roll(x, shift, 1) if shift else x
                    outs[s] = y if u == 0 else jnp.where(keep, y, outs[s])
            for s in range(slabs):
                dst_ref[k * slabs + s, :, pl.ds(w * 128, 128)] = outs[s]


def regroup(got):
    count, piece, lanes = got.shape
    width = lanes // count
    nbytes = got.size * got.dtype.itemsize
    return pl.pallas_call(
        _gather_kernel,
        in_specs=[pl.BlockSpec(memory_space=pltpu.VMEM)],
        out_specs=pl.BlockSpec(memory_space=pltpu.VMEM),
        out_shape=jax.ShapeDtypeStruct((lanes // width, piece, count * width), got.dtype),
        cost_estimate=pl.CostEstimate(flops=0, transcendentals=0, bytes_accessed=2 * nbytes),
    )(got)


def flipped(stacked):
    ages, states, rows, lanes = stacked.shape
    count = lax.axis_size("asset")
    piece = lanes // count
    flat = stacked.reshape(ages * states * rows, lanes).T.reshape(count, piece, ages * states * rows)
    got = lax.all_to_all(flat, "asset", 0, 0, tiled=True)
    return regroup(got).reshape(ages, states, piece, count * rows)


def local(
    values,
    utility,
    earn_prob,
    support_start,
    liquid_offset,
    liquid_weight,
    illiquid_offset,
    illiquid_weight,
):
    liquid_map = band_matrix(liquid_offset, liquid_weight)
    illiquid_map = band_matrix(illiquid_offset, illiquid_weight)

    expected = continuation(values, earn_prob, support_start)
    saved = along_lanes(expected, liquid_map)
    adjusted = along_lanes(flipped(saved), illiquid_map)
    current = flipped(utility) + DISCOUNT * adjusted

    expected = continuation(current, earn_prob, support_start)
    moved = along_lanes(expected, illiquid_map)
    adjusted = along_lanes(flipped(moved), liquid_map)
    return utility + DISCOUNT * adjusted


def solution(mesh):
    return jax.shard_map(
        local,
        mesh=mesh,
        in_specs=(
            P("age", "earn", "asset", None),
            P("age", "earn", "asset", None),
            P(None, "earn"),
            P("earn"),
            P("earn", None),
            P(None, "earn", None),
            P("earn", None),
            P(None, "earn", None),
        ),
        out_specs=P("age", "earn", "asset", None),
        check_vma=False,
    )
```

```python
import jax
import jax.numpy as jnp
from jax import lax
from jax.experimental import pallas as pl
from jax.experimental.pallas import tpu as pltpu
from jax.sharding import PartitionSpec as P

REACH = 4
BAND = 4
ITERS = 2


DISCOUNT = 0.96
PRECISE = lax.Precision.HIGHEST


def band_matrix(offset, weight):
    extent = offset.shape[1]
    positions = jnp.arange(extent, dtype=jnp.int32)
    matrix = jnp.zeros((offset.shape[0], extent, extent), jnp.float32)
    for number in range(BAND):
        matrix = matrix + jnp.where(
            positions[None, :, None] == (offset + number)[:, None, :],
            weight[number][:, None, :],
            0.0,
        )
    return matrix


def neighbours(current):
    states = current.shape[1]
    ages = lax.axis_size("age")
    earns = lax.axis_size("earn")
    axes = ("earn", "age")

    def moved(value, by_earn, by_age):
        pairs = []
        for e in range(earns):
            for a in range(ages):
                te, ta = e + by_earn, a + by_age
                if 0 <= te < earns and 0 <= ta < ages:
                    pairs.append((e * ages + a, te * ages + ta))
        return lax.ppermute(value, axes, pairs)

    head = slice(0, REACH)
    tail = slice(states - REACH, states)
    here = jnp.concatenate(
        [moved(current[1:, tail], 1, 0), current[1:], moved(current[1:, head], -1, 0)], axis=1
    )
    above = jnp.concatenate(
        [moved(current[:1, tail], 1, -1), moved(current[:1], 0, -1), moved(current[:1, head], -1, -1)],
        axis=1,
    )
    return jnp.concatenate([here, above], axis=0)


def continuation(current, earn_prob, support_start):
    padded = neighbours(current)
    states_here = current.shape[1]
    first_state = lax.axis_index("earn") * states_here
    slots = jnp.arange(states_here + 2 * REACH, dtype=jnp.int32)
    prob_sum = jnp.sum(earn_prob, axis=0)
    mixing = jnp.zeros((states_here, states_here + 2 * REACH), jnp.float32)
    for number in range(REACH + 1):
        target = support_start + number - first_state + REACH
        mixing = mixing + jnp.where(
            slots[None, :] == target[:, None], (earn_prob[number] / prob_sum)[:, None], 0.0
        )
    return jnp.einsum("ij,tjxy->tixy", mixing, padded, precision=lax.Precision.HIGH)


def along_lanes(stacked, matrix):
    return jnp.einsum("terc,ecn->tern", stacked, matrix, precision=lax.Precision.HIGH)


def _gather_kernel(src_ref, dst_ref):
    count, piece, lanes = src_ref.shape
    width = dst_ref.shape[2] // count
    slabs = 128 // width
    lane = lax.broadcasted_iota(jnp.int32, (piece, 128), 1)
    for k in range(lanes // 128):
        for w in range(count // slabs):
            outs = [None] * slabs
            for u in range(slabs):
                x = src_ref[w * slabs + u, :, pl.ds(k * 128, 128)]
                keep = (lane >= u * width) & (lane < (u + 1) * width)
                for s in range(slabs):
                    shift = ((u - s) * width) % 128
                    y = pltpu.roll(x, shift, 1) if shift else x
                    outs[s] = y if u == 0 else jnp.where(keep, y, outs[s])
            for s in range(slabs):
                dst_ref[k * slabs + s, :, pl.ds(w * 128, 128)] = outs[s]


def regroup(got):
    count, piece, lanes = got.shape
    width = lanes // count
    nbytes = got.size * got.dtype.itemsize
    return pl.pallas_call(
        _gather_kernel,
        in_specs=[pl.BlockSpec(memory_space=pltpu.VMEM)],
        out_specs=pl.BlockSpec(memory_space=pltpu.VMEM),
        out_shape=jax.ShapeDtypeStruct((lanes // width, piece, count * width), got.dtype),
        cost_estimate=pl.CostEstimate(flops=0, transcendentals=0, bytes_accessed=2 * nbytes),
    )(got)


def flipped(stacked):
    ages, states, rows, lanes = stacked.shape
    count = lax.axis_size("asset")
    piece = lanes // count
    flat = stacked.reshape(ages * states * rows, lanes).T.reshape(count, piece, ages * states * rows)
    got = lax.all_to_all(flat, "asset", 0, 0, tiled=True)
    return regroup(got).reshape(ages, states, piece, count * rows)


def local(
    values,
    utility,
    earn_prob,
    support_start,
    liquid_offset,
    liquid_weight,
    illiquid_offset,
    illiquid_weight,
):
    expected = continuation(values, earn_prob, support_start)
    saved = along_lanes(expected, band_matrix(liquid_offset, liquid_weight))
    saved, illiquid_offset, illiquid_weight = lax.optimization_barrier(
        (saved, illiquid_offset, illiquid_weight)
    )
    illiquid_map = lax.optimization_barrier(band_matrix(illiquid_offset, illiquid_weight))
    adjusted = along_lanes(flipped(saved), illiquid_map)
    current = flipped(utility) + DISCOUNT * adjusted
    current, liquid_offset, liquid_weight = lax.optimization_barrier(
        (current, liquid_offset, liquid_weight)
    )
    liquid_map = lax.optimization_barrier(band_matrix(liquid_offset, liquid_weight))

    expected = continuation(current, earn_prob, support_start)
    moved = along_lanes(expected, illiquid_map)
    adjusted = along_lanes(flipped(moved), liquid_map)
    return utility + DISCOUNT * adjusted


def solution(mesh):
    return jax.shard_map(
        local,
        mesh=mesh,
        in_specs=(
            P("age", "earn", "asset", None),
            P("age", "earn", "asset", None),
            P(None, "earn"),
            P("earn"),
            P("earn", None),
            P(None, "earn", None),
            P("earn", None),
            P(None, "earn", None),
        ),
        out_specs=P("age", "earn", "asset", None),
        check_vma=False,
    )
```

```python
import jax
import jax.numpy as jnp
from jax import lax
from jax.experimental import pallas as pl
from jax.experimental.pallas import tpu as pltpu
from jax.sharding import PartitionSpec as P

REACH = 4
BAND = 4
ITERS = 2


DISCOUNT = 0.96
PRECISE = lax.Precision.HIGHEST


def band_matrix(offset, weight):
    extent = offset.shape[1]
    positions = jnp.arange(extent, dtype=jnp.int32)
    matrix = jnp.zeros((offset.shape[0], extent, extent), jnp.float32)
    for number in range(BAND):
        matrix = matrix + jnp.where(
            positions[None, :, None] == (offset + number)[:, None, :],
            weight[number][:, None, :],
            0.0,
        )
    return matrix


def neighbours(current):
    states = current.shape[1]
    ages = lax.axis_size("age")
    earns = lax.axis_size("earn")
    axes = ("earn", "age")

    def moved(value, by_earn, by_age):
        pairs = []
        for e in range(earns):
            for a in range(ages):
                te, ta = e + by_earn, a + by_age
                if 0 <= te < earns and 0 <= ta < ages:
                    pairs.append((e * ages + a, te * ages + ta))
        return lax.ppermute(value, axes, pairs)

    head = slice(0, REACH)
    tail = slice(states - REACH, states)
    here = jnp.concatenate(
        [moved(current[1:, tail], 1, 0), current[1:], moved(current[1:, head], -1, 0)], axis=1
    )
    above = jnp.concatenate(
        [moved(current[:1, tail], 1, -1), moved(current[:1], 0, -1), moved(current[:1, head], -1, -1)],
        axis=1,
    )
    return jnp.concatenate([here, above], axis=0)


def continuation(current, earn_prob, support_start):
    padded = neighbours(current)
    states_here = current.shape[1]
    first_state = lax.axis_index("earn") * states_here
    slots = jnp.arange(states_here + 2 * REACH, dtype=jnp.int32)
    prob_sum = jnp.sum(earn_prob, axis=0)
    mixing = jnp.zeros((states_here, states_here + 2 * REACH), jnp.float32)
    for number in range(REACH + 1):
        target = support_start + number - first_state + REACH
        mixing = mixing + jnp.where(
            slots[None, :] == target[:, None], (earn_prob[number] / prob_sum)[:, None], 0.0
        )
    return jnp.einsum("ij,tjxy->tixy", mixing, padded, precision=lax.Precision.HIGH)


def along_lanes(stacked, matrix):
    return jnp.einsum("terc,ecn->tern", stacked, matrix, precision=lax.Precision.HIGH)


def _gather_kernel(src_ref, dst_ref):
    count, piece, lanes = src_ref.shape
    width = dst_ref.shape[2] // count
    slabs = 128 // width
    lane = lax.broadcasted_iota(jnp.int32, (piece, 128), 1)
    for k in range(lanes // 128):
        for w in range(count // slabs):
            outs = [None] * slabs
            for u in range(slabs):
                x = src_ref[w * slabs + u, :, pl.ds(k * 128, 128)]
                keep = (lane >= u * width) & (lane < (u + 1) * width)
                for s in range(slabs):
                    shift = ((u - s) * width) % 128
                    y = pltpu.roll(x, shift, 1) if shift else x
                    outs[s] = y if u == 0 else jnp.where(keep, y, outs[s])
            for s in range(slabs):
                dst_ref[k * slabs + s, :, pl.ds(w * 128, 128)] = outs[s]


def regroup(got):
    count, piece, lanes = got.shape
    width = lanes // count
    nbytes = got.size * got.dtype.itemsize
    return pl.pallas_call(
        _gather_kernel,
        in_specs=[pl.BlockSpec(memory_space=pltpu.VMEM)],
        out_specs=pl.BlockSpec(memory_space=pltpu.VMEM),
        out_shape=jax.ShapeDtypeStruct((lanes // width, piece, count * width), got.dtype),
        cost_estimate=pl.CostEstimate(flops=0, transcendentals=0, bytes_accessed=2 * nbytes),
    )(got)


def flipped(stacked):
    ages, states, rows, lanes = stacked.shape
    count = lax.axis_size("asset")
    piece = lanes // count
    flat = stacked.reshape(ages * states * rows, lanes).T.reshape(count, piece, ages * states * rows)
    got = lax.all_to_all(flat, "asset", 0, 0, tiled=True)
    return regroup(got).reshape(ages, states, piece, count * rows)


def local(
    values,
    utility,
    earn_prob,
    support_start,
    liquid_offset,
    liquid_weight,
    illiquid_offset,
    illiquid_weight,
):
    expected = continuation(values, earn_prob, support_start)
    saved = along_lanes(expected, band_matrix(liquid_offset, liquid_weight))
    saved, illiquid_offset, illiquid_weight, liquid_offset, liquid_weight = lax.optimization_barrier(
        (saved, illiquid_offset, illiquid_weight, liquid_offset, liquid_weight)
    )
    illiquid_map, liquid_map = lax.optimization_barrier(
        (band_matrix(illiquid_offset, illiquid_weight), band_matrix(liquid_offset, liquid_weight))
    )
    adjusted = along_lanes(flipped(saved), illiquid_map)
    current = flipped(utility) + DISCOUNT * adjusted

    expected = continuation(current, earn_prob, support_start)
    moved = along_lanes(expected, illiquid_map)
    adjusted = along_lanes(flipped(moved), liquid_map)
    return utility + DISCOUNT * adjusted


def solution(mesh):
    return jax.shard_map(
        local,
        mesh=mesh,
        in_specs=(
            P("age", "earn", "asset", None),
            P("age", "earn", "asset", None),
            P(None, "earn"),
            P("earn"),
            P("earn", None),
            P(None, "earn", None),
            P("earn", None),
            P(None, "earn", None),
        ),
        out_specs=P("age", "earn", "asset", None),
        check_vma=False,
    )
```

```python
import jax
import jax.numpy as jnp
from jax import lax
from jax.experimental import pallas as pl
from jax.experimental.pallas import tpu as pltpu
from jax.sharding import PartitionSpec as P

REACH = 4
BAND = 4
ITERS = 2


DISCOUNT = 0.96
PRECISE = lax.Precision.HIGHEST


def band_matrix(offset, weight):
    extent = offset.shape[1]
    positions = jnp.arange(extent, dtype=jnp.int32)
    matrix = jnp.zeros((offset.shape[0], extent, extent), jnp.float32)
    for number in range(BAND):
        matrix = matrix + jnp.where(
            positions[None, :, None] == (offset + number)[:, None, :],
            weight[number][:, None, :],
            0.0,
        )
    return matrix


def neighbours(current):
    states = current.shape[1]
    ages = lax.axis_size("age")
    earns = lax.axis_size("earn")
    axes = ("earn", "age")

    def moved(value, by_earn, by_age):
        pairs = []
        for e in range(earns):
            for a in range(ages):
                te, ta = e + by_earn, a + by_age
                if 0 <= te < earns and 0 <= ta < ages:
                    pairs.append((e * ages + a, te * ages + ta))
        return lax.ppermute(value, axes, pairs)

    head = slice(0, REACH)
    tail = slice(states - REACH, states)
    here = jnp.concatenate(
        [moved(current[1:, tail], 1, 0), current[1:], moved(current[1:, head], -1, 0)], axis=1
    )
    above = jnp.concatenate(
        [moved(current[:1, tail], 1, -1), moved(current[:1], 0, -1), moved(current[:1, head], -1, -1)],
        axis=1,
    )
    return here, above


def continuation(current, earn_prob, support_start):
    return jnp.concatenate(mixed(current, earn_prob, support_start), axis=0)


def mixed(current, earn_prob, support_start):
    chunks = neighbours(current)
    states_here = current.shape[1]
    first_state = lax.axis_index("earn") * states_here
    slots = jnp.arange(states_here + 2 * REACH, dtype=jnp.int32)
    prob_sum = jnp.sum(earn_prob, axis=0)
    mixing = jnp.zeros((states_here, states_here + 2 * REACH), jnp.float32)
    for number in range(REACH + 1):
        target = support_start + number - first_state + REACH
        mixing = mixing + jnp.where(
            slots[None, :] == target[:, None], (earn_prob[number] / prob_sum)[:, None], 0.0
        )
    return tuple(
        jnp.einsum("ij,tjxy->tixy", mixing, padded, precision=lax.Precision.HIGH) for padded in chunks
    )


def along_lanes(stacked, matrix):
    return jnp.einsum("terc,ecn->tern", stacked, matrix, precision=lax.Precision.HIGH)


def _gather_kernel(src_ref, dst_ref):
    count, piece, lanes = src_ref.shape
    width = dst_ref.shape[2] // count
    slabs = 128 // width
    lane = lax.broadcasted_iota(jnp.int32, (piece, 128), 1)
    for k in range(lanes // 128):
        for w in range(count // slabs):
            outs = [None] * slabs
            for u in range(slabs):
                x = src_ref[w * slabs + u, :, pl.ds(k * 128, 128)]
                keep = (lane >= u * width) & (lane < (u + 1) * width)
                for s in range(slabs):
                    shift = ((u - s) * width) % 128
                    y = pltpu.roll(x, shift, 1) if shift else x
                    outs[s] = y if u == 0 else jnp.where(keep, y, outs[s])
            for s in range(slabs):
                dst_ref[k * slabs + s, :, pl.ds(w * 128, 128)] = outs[s]


def regroup(got, width):
    count, piece, lanes = got.shape
    nbytes = got.size * got.dtype.itemsize
    return pl.pallas_call(
        _gather_kernel,
        in_specs=[pl.BlockSpec(memory_space=pltpu.VMEM)],
        out_specs=pl.BlockSpec(memory_space=pltpu.VMEM),
        out_shape=jax.ShapeDtypeStruct((lanes // width, piece, count * width), got.dtype),
        cost_estimate=pl.CostEstimate(flops=0, transcendentals=0, bytes_accessed=2 * nbytes),
    )(got)


def flipped(stacked):
    ages, states, rows, lanes = stacked.shape
    count = lax.axis_size("asset")
    piece = lanes // count
    flat = stacked.reshape(ages * states * rows, lanes).T.reshape(count, piece, ages * states * rows)
    got = lax.all_to_all(flat, "asset", 0, 0, tiled=True)
    return regroup(got, rows).reshape(ages, states, piece, count * rows)


def local(
    values,
    utility,
    earn_prob,
    support_start,
    liquid_offset,
    liquid_weight,
    illiquid_offset,
    illiquid_weight,
):
    expected = continuation(values, earn_prob, support_start)
    saved = along_lanes(expected, band_matrix(liquid_offset, liquid_weight))
    saved, illiquid_offset, illiquid_weight, liquid_offset, liquid_weight = lax.optimization_barrier(
        (saved, illiquid_offset, illiquid_weight, liquid_offset, liquid_weight)
    )
    illiquid_map, liquid_map = lax.optimization_barrier(
        (band_matrix(illiquid_offset, illiquid_weight), band_matrix(liquid_offset, liquid_weight))
    )
    adjusted = along_lanes(flipped(saved), illiquid_map)
    current = flipped(utility) + DISCOUNT * adjusted

    back = [flipped(along_lanes(part, illiquid_map)) for part in mixed(current, earn_prob, support_start)]
    adjusted = along_lanes(jnp.concatenate(back, axis=0), liquid_map)
    return utility + DISCOUNT * adjusted


def solution(mesh):
    return jax.shard_map(
        local,
        mesh=mesh,
        in_specs=(
            P("age", "earn", "asset", None),
            P("age", "earn", "asset", None),
            P(None, "earn"),
            P("earn"),
            P("earn", None),
            P(None, "earn", None),
            P("earn", None),
            P(None, "earn", None),
        ),
        out_specs=P("age", "earn", "asset", None),
        check_vma=False,
    )
```

```python
import jax
import jax.numpy as jnp
from jax import lax
from jax.experimental import pallas as pl
from jax.experimental.pallas import tpu as pltpu
from jax.sharding import PartitionSpec as P

REACH = 4
BAND = 4
ITERS = 2


DISCOUNT = 0.96
PRECISE = lax.Precision.HIGHEST


def band_matrix(offset, weight):
    extent = offset.shape[1]
    positions = jnp.arange(extent, dtype=jnp.int32)
    matrix = jnp.zeros((offset.shape[0], extent, extent), jnp.float32)
    for number in range(BAND):
        matrix = matrix + jnp.where(
            positions[None, :, None] == (offset + number)[:, None, :],
            weight[number][:, None, :],
            0.0,
        )
    return matrix


def neighbours(current):
    states = current.shape[1]
    ages = lax.axis_size("age")
    earns = lax.axis_size("earn")
    axes = ("earn", "age")

    def moved(value, by_earn, by_age):
        pairs = []
        for e in range(earns):
            for a in range(ages):
                te, ta = e + by_earn, a + by_age
                if 0 <= te < earns and 0 <= ta < ages:
                    pairs.append((e * ages + a, te * ages + ta))
        return lax.ppermute(value, axes, pairs)

    head = slice(0, REACH)
    tail = slice(states - REACH, states)
    here = jnp.concatenate(
        [moved(current[1:, tail], 1, 0), current[1:], moved(current[1:, head], -1, 0)], axis=1
    )
    above = jnp.concatenate(
        [moved(current[:1, tail], 1, -1), moved(current[:1], 0, -1), moved(current[:1, head], -1, -1)],
        axis=1,
    )
    return jnp.concatenate([here, above], axis=0)


def continuation(current, earn_prob, support_start):
    return mix(neighbours(current), earn_prob, support_start)


def mix(padded, earn_prob, support_start):
    states_here = padded.shape[1] - 2 * REACH
    first_state = lax.axis_index("earn") * states_here
    slots = jnp.arange(states_here + 2 * REACH, dtype=jnp.int32)
    prob_sum = jnp.sum(earn_prob, axis=0)
    mixing = jnp.zeros((states_here, states_here + 2 * REACH), jnp.float32)
    for number in range(REACH + 1):
        target = support_start + number - first_state + REACH
        mixing = mixing + jnp.where(
            slots[None, :] == target[:, None], (earn_prob[number] / prob_sum)[:, None], 0.0
        )
    return jnp.einsum("ij,tjxy->tixy", mixing, padded, precision=lax.Precision.HIGH)


def along_lanes(stacked, matrix):
    return jnp.einsum("terc,ecn->tern", stacked, matrix, precision=lax.Precision.HIGH)


def _gather_kernel(src_ref, dst_ref):
    count, piece, lanes = src_ref.shape
    width = dst_ref.shape[2] // count
    slabs = 128 // width
    lane = lax.broadcasted_iota(jnp.int32, (piece, 128), 1)
    for k in range(lanes // 128):
        for w in range(count // slabs):
            outs = [None] * slabs
            for u in range(slabs):
                x = src_ref[w * slabs + u, :, pl.ds(k * 128, 128)]
                keep = (lane >= u * width) & (lane < (u + 1) * width)
                for s in range(slabs):
                    shift = ((u - s) * width) % 128
                    y = pltpu.roll(x, shift, 1) if shift else x
                    outs[s] = y if u == 0 else jnp.where(keep, y, outs[s])
            for s in range(slabs):
                dst_ref[k * slabs + s, :, pl.ds(w * 128, 128)] = outs[s]


def regroup(got):
    count, piece, lanes = got.shape
    width = lanes // count
    nbytes = got.size * got.dtype.itemsize
    return pl.pallas_call(
        _gather_kernel,
        in_specs=[pl.BlockSpec(memory_space=pltpu.VMEM)],
        out_specs=pl.BlockSpec(memory_space=pltpu.VMEM),
        out_shape=jax.ShapeDtypeStruct((lanes // width, piece, count * width), got.dtype),
        cost_estimate=pl.CostEstimate(flops=0, transcendentals=0, bytes_accessed=2 * nbytes),
    )(got)


def flipped(stacked):
    ages, states, rows, lanes = stacked.shape
    count = lax.axis_size("asset")
    piece = lanes // count
    flat = stacked.reshape(ages * states * rows, lanes).T.reshape(count, piece, ages * states * rows)
    got = lax.all_to_all(flat, "asset", 0, 0, tiled=True)
    return regroup(got).reshape(ages, states, piece, count * rows)


def local(
    values,
    utility,
    earn_prob,
    support_start,
    liquid_offset,
    liquid_weight,
    illiquid_offset,
    illiquid_weight,
):
    padded, utility = lax.optimization_barrier((neighbours(values), utility))
    expected = mix(padded, earn_prob, support_start)
    saved = along_lanes(expected, band_matrix(liquid_offset, liquid_weight))
    saved, illiquid_offset, illiquid_weight, liquid_offset, liquid_weight = lax.optimization_barrier(
        (saved, illiquid_offset, illiquid_weight, liquid_offset, liquid_weight)
    )
    illiquid_map, liquid_map = lax.optimization_barrier(
        (band_matrix(illiquid_offset, illiquid_weight), band_matrix(liquid_offset, liquid_weight))
    )
    adjusted = along_lanes(flipped(saved), illiquid_map)
    current = flipped(utility) + DISCOUNT * adjusted

    expected = continuation(current, earn_prob, support_start)
    moved = along_lanes(expected, illiquid_map)
    adjusted = along_lanes(flipped(moved), liquid_map)
    return utility + DISCOUNT * adjusted


def solution(mesh):
    return jax.shard_map(
        local,
        mesh=mesh,
        in_specs=(
            P("age", "earn", "asset", None),
            P("age", "earn", "asset", None),
            P(None, "earn"),
            P("earn"),
            P("earn", None),
            P(None, "earn", None),
            P("earn", None),
            P(None, "earn", None),
        ),
        out_specs=P("age", "earn", "asset", None),
        check_vma=False,
    )
```

```python
import jax
import jax.numpy as jnp
from jax import lax
from jax.experimental import pallas as pl
from jax.experimental.pallas import tpu as pltpu
from jax.sharding import PartitionSpec as P

REACH = 4
BAND = 4
ITERS = 2


DISCOUNT = 0.96
PRECISE = lax.Precision.HIGHEST


def band_matrix(offset, weight):
    extent = offset.shape[1]
    positions = jnp.arange(extent, dtype=jnp.int32)
    matrix = jnp.zeros((offset.shape[0], extent, extent), jnp.float32)
    for number in range(BAND):
        matrix = matrix + jnp.where(
            positions[None, :, None] == (offset + number)[:, None, :],
            weight[number][:, None, :],
            0.0,
        )
    return matrix


def neighbours(current):
    states = current.shape[1]
    ages = lax.axis_size("age")
    earns = lax.axis_size("earn")
    axes = ("earn", "age")

    def moved(value, by_earn, by_age):
        pairs = []
        for e in range(earns):
            for a in range(ages):
                te, ta = e + by_earn, a + by_age
                if 0 <= te < earns and 0 <= ta < ages:
                    pairs.append((e * ages + a, te * ages + ta))
        return lax.ppermute(value, axes, pairs)

    head = slice(0, REACH)
    tail = slice(states - REACH, states)
    here = jnp.concatenate(
        [moved(current[1:, tail], 1, 0), current[1:], moved(current[1:, head], -1, 0)], axis=1
    )
    above = jnp.concatenate(
        [moved(current[:1, tail], 1, -1), moved(current[:1], 0, -1), moved(current[:1, head], -1, -1)],
        axis=1,
    )
    return here, above


def continuation(current, earn_prob, support_start):
    return jnp.concatenate([mix(part, earn_prob, support_start) for part in neighbours(current)], axis=0)


def mix(padded, earn_prob, support_start):
    states_here = padded.shape[1] - 2 * REACH
    first_state = lax.axis_index("earn") * states_here
    slots = jnp.arange(states_here + 2 * REACH, dtype=jnp.int32)
    prob_sum = jnp.sum(earn_prob, axis=0)
    mixing = jnp.zeros((states_here, states_here + 2 * REACH), jnp.float32)
    for number in range(REACH + 1):
        target = support_start + number - first_state + REACH
        mixing = mixing + jnp.where(
            slots[None, :] == target[:, None], (earn_prob[number] / prob_sum)[:, None], 0.0
        )
    return jnp.einsum("ij,tjxy->tixy", mixing, padded, precision=lax.Precision.HIGH)


def along_lanes(stacked, matrix):
    return jnp.einsum("terc,ecn->tern", stacked, matrix, precision=lax.Precision.HIGH)


def _gather_kernel(src_ref, dst_ref):
    count, piece, lanes = src_ref.shape
    width = dst_ref.shape[2] // count
    slabs = 128 // width
    lane = lax.broadcasted_iota(jnp.int32, (piece, 128), 1)
    for k in range(lanes // 128):
        for w in range(count // slabs):
            outs = [None] * slabs
            for u in range(slabs):
                x = src_ref[w * slabs + u, :, pl.ds(k * 128, 128)]
                keep = (lane >= u * width) & (lane < (u + 1) * width)
                for s in range(slabs):
                    shift = ((u - s) * width) % 128
                    y = pltpu.roll(x, shift, 1) if shift else x
                    outs[s] = y if u == 0 else jnp.where(keep, y, outs[s])
            for s in range(slabs):
                dst_ref[k * slabs + s, :, pl.ds(w * 128, 128)] = outs[s]


def regroup(got):
    count, piece, lanes = got.shape
    width = lanes // count
    nbytes = got.size * got.dtype.itemsize
    return pl.pallas_call(
        _gather_kernel,
        in_specs=[pl.BlockSpec(memory_space=pltpu.VMEM)],
        out_specs=pl.BlockSpec(memory_space=pltpu.VMEM),
        out_shape=jax.ShapeDtypeStruct((lanes // width, piece, count * width), got.dtype),
        cost_estimate=pl.CostEstimate(flops=0, transcendentals=0, bytes_accessed=2 * nbytes),
    )(got)


def flipped(stacked):
    ages, states, rows, lanes = stacked.shape
    count = lax.axis_size("asset")
    piece = lanes // count
    flat = stacked.reshape(ages * states * rows, lanes).T.reshape(count, piece, ages * states * rows)
    got = lax.all_to_all(flat, "asset", 0, 0, tiled=True)
    return regroup(got).reshape(ages, states, piece, count * rows)


def local(
    values,
    utility,
    earn_prob,
    support_start,
    liquid_offset,
    liquid_weight,
    illiquid_offset,
    illiquid_weight,
):
    liquid_map = lax.optimization_barrier(band_matrix(liquid_offset, liquid_weight))
    saved = jnp.concatenate(
        [along_lanes(mix(part, earn_prob, support_start), liquid_map) for part in neighbours(values)], axis=0
    )
    saved, illiquid_offset, illiquid_weight = lax.optimization_barrier(
        (saved, illiquid_offset, illiquid_weight)
    )
    illiquid_map = lax.optimization_barrier(band_matrix(illiquid_offset, illiquid_weight))
    adjusted = along_lanes(flipped(saved), illiquid_map)
    current = flipped(utility) + DISCOUNT * adjusted

    expected = continuation(current, earn_prob, support_start)
    moved = along_lanes(expected, illiquid_map)
    adjusted = along_lanes(flipped(moved), liquid_map)
    return utility + DISCOUNT * adjusted


def solution(mesh):
    return jax.shard_map(
        local,
        mesh=mesh,
        in_specs=(
            P("age", "earn", "asset", None),
            P("age", "earn", "asset", None),
            P(None, "earn"),
            P("earn"),
            P("earn", None),
            P(None, "earn", None),
            P("earn", None),
            P(None, "earn", None),
        ),
        out_specs=P("age", "earn", "asset", None),
        check_vma=False,
    )
```

```python
import jax
import jax.numpy as jnp
from jax import lax
from jax.experimental import pallas as pl
from jax.experimental.pallas import tpu as pltpu
from jax.sharding import PartitionSpec as P

REACH = 4
BAND = 4
ITERS = 2


DISCOUNT = 0.96
PRECISE = lax.Precision.HIGHEST


def band_matrix(offset, weight):
    extent = offset.shape[1]
    positions = jnp.arange(extent, dtype=jnp.int32)
    matrix = jnp.zeros((offset.shape[0], extent, extent), jnp.float32)
    for number in range(BAND):
        matrix = matrix + jnp.where(
            positions[None, :, None] == (offset + number)[:, None, :],
            weight[number][:, None, :],
            0.0,
        )
    return matrix


def neighbours(current):
    states = current.shape[1]
    ages = lax.axis_size("age")
    earns = lax.axis_size("earn")
    axes = ("earn", "age")

    def moved(value, by_earn, by_age):
        pairs = []
        for e in range(earns):
            for a in range(ages):
                te, ta = e + by_earn, a + by_age
                if 0 <= te < earns and 0 <= ta < ages:
                    pairs.append((e * ages + a, te * ages + ta))
        return lax.ppermute(value, axes, pairs)

    head = slice(0, REACH)
    tail = slice(states - REACH, states)
    here = jnp.concatenate(
        [moved(current[1:, tail], 1, 0), current[1:], moved(current[1:, head], -1, 0)], axis=1
    )
    above = jnp.concatenate(
        [moved(current[:1, tail], 1, -1), moved(current[:1], 0, -1), moved(current[:1, head], -1, -1)],
        axis=1,
    )
    return here, above


def continuation(current, earn_prob, support_start):
    return jnp.concatenate([mix(part, earn_prob, support_start) for part in neighbours(current)], axis=0)


def mix(padded, earn_prob, support_start):
    states_here = padded.shape[1] - 2 * REACH
    first_state = lax.axis_index("earn") * states_here
    slots = jnp.arange(states_here + 2 * REACH, dtype=jnp.int32)
    prob_sum = jnp.sum(earn_prob, axis=0)
    mixing = jnp.zeros((states_here, states_here + 2 * REACH), jnp.float32)
    for number in range(REACH + 1):
        target = support_start + number - first_state + REACH
        mixing = mixing + jnp.where(
            slots[None, :] == target[:, None], (earn_prob[number] / prob_sum)[:, None], 0.0
        )
    return jnp.einsum("ij,tjxy->tixy", mixing, padded, precision=lax.Precision.HIGH)


def along_lanes(stacked, matrix):
    return jnp.einsum("terc,ecn->tern", stacked, matrix, precision=lax.Precision.HIGH)


def _gather_kernel(src_ref, dst_ref):
    count, piece, lanes = src_ref.shape
    width = dst_ref.shape[2] // count
    slabs = 128 // width
    lane = lax.broadcasted_iota(jnp.int32, (piece, 128), 1)
    for k in range(lanes // 128):
        for w in range(count // slabs):
            outs = [None] * slabs
            for u in range(slabs):
                x = src_ref[w * slabs + u, :, pl.ds(k * 128, 128)]
                keep = (lane >= u * width) & (lane < (u + 1) * width)
                for s in range(slabs):
                    shift = ((u - s) * width) % 128
                    y = pltpu.roll(x, shift, 1) if shift else x
                    outs[s] = y if u == 0 else jnp.where(keep, y, outs[s])
            for s in range(slabs):
                dst_ref[k * slabs + s, :, pl.ds(w * 128, 128)] = outs[s]


def regroup(got):
    count, piece, lanes = got.shape
    width = lanes // count
    nbytes = got.size * got.dtype.itemsize
    return pl.pallas_call(
        _gather_kernel,
        in_specs=[pl.BlockSpec(memory_space=pltpu.VMEM)],
        out_specs=pl.BlockSpec(memory_space=pltpu.VMEM),
        out_shape=jax.ShapeDtypeStruct((lanes // width, piece, count * width), got.dtype),
        cost_estimate=pl.CostEstimate(flops=0, transcendentals=0, bytes_accessed=2 * nbytes),
    )(got)


def flipped(stacked):
    ages, states, rows, lanes = stacked.shape
    count = lax.axis_size("asset")
    piece = lanes // count
    flat = stacked.reshape(ages * states * rows, lanes).T.reshape(count, piece, ages * states * rows)
    got = lax.all_to_all(flat, "asset", 0, 0, tiled=True)
    return regroup(got).reshape(ages, states, piece, count * rows)


def local(
    values,
    utility,
    earn_prob,
    support_start,
    liquid_offset,
    liquid_weight,
    illiquid_offset,
    illiquid_weight,
):
    liquid_map = lax.optimization_barrier(band_matrix(liquid_offset, liquid_weight))
    saved = jnp.concatenate(
        [along_lanes(mix(part, earn_prob, support_start), liquid_map) for part in neighbours(values)], axis=0
    )
    saved, illiquid_offset, illiquid_weight = lax.optimization_barrier(
        (saved, illiquid_offset, illiquid_weight)
    )
    illiquid_map = lax.optimization_barrier(band_matrix(illiquid_offset, illiquid_weight))
    adjusted = along_lanes(flipped(saved), illiquid_map)
    current = flipped(utility) + DISCOUNT * adjusted

    moved = jnp.concatenate(
        [along_lanes(mix(part, earn_prob, support_start), illiquid_map) for part in neighbours(current)], axis=0
    )
    adjusted = along_lanes(flipped(moved), liquid_map)
    return utility + DISCOUNT * adjusted


def solution(mesh):
    return jax.shard_map(
        local,
        mesh=mesh,
        in_specs=(
            P("age", "earn", "asset", None),
            P("age", "earn", "asset", None),
            P(None, "earn"),
            P("earn"),
            P("earn", None),
            P(None, "earn", None),
            P("earn", None),
            P(None, "earn", None),
        ),
        out_specs=P("age", "earn", "asset", None),
        check_vma=False,
    )
```

```python
import jax
import jax.numpy as jnp
from jax import lax
from jax.experimental import pallas as pl
from jax.experimental.pallas import tpu as pltpu
from jax.sharding import PartitionSpec as P

REACH = 4
BAND = 4
ITERS = 2


DISCOUNT = 0.96
PRECISE = lax.Precision.HIGHEST


def band_matrix(offset, weight):
    extent = offset.shape[1]
    positions = jnp.arange(extent, dtype=jnp.int32)
    matrix = jnp.zeros((offset.shape[0], extent, extent), jnp.float32)
    for number in range(BAND):
        matrix = matrix + jnp.where(
            positions[None, :, None] == (offset + number)[:, None, :],
            weight[number][:, None, :],
            0.0,
        )
    return matrix


def neighbours(current):
    states = current.shape[1]
    ages = lax.axis_size("age")
    earns = lax.axis_size("earn")
    axes = ("earn", "age")

    def moved(value, by_earn, by_age):
        pairs = []
        for e in range(earns):
            for a in range(ages):
                te, ta = e + by_earn, a + by_age
                if 0 <= te < earns and 0 <= ta < ages:
                    pairs.append((e * ages + a, te * ages + ta))
        return lax.ppermute(value, axes, pairs)

    head = slice(0, REACH)
    tail = slice(states - REACH, states)
    here = jnp.concatenate(
        [moved(current[1:, tail], 1, 0), current[1:], moved(current[1:, head], -1, 0)], axis=1
    )
    above = jnp.concatenate(
        [moved(current[:1, tail], 1, -1), moved(current[:1], 0, -1), moved(current[:1, head], -1, -1)],
        axis=1,
    )
    return here, above


def continuation(current, earn_prob, support_start):
    return jnp.concatenate([mix(part, earn_prob, support_start) for part in neighbours(current)], axis=0)


def mix(padded, earn_prob, support_start):
    states_here = padded.shape[1] - 2 * REACH
    first_state = lax.axis_index("earn") * states_here
    slots = jnp.arange(states_here + 2 * REACH, dtype=jnp.int32)
    prob_sum = jnp.sum(earn_prob, axis=0)
    mixing = jnp.zeros((states_here, states_here + 2 * REACH), jnp.float32)
    for number in range(REACH + 1):
        target = support_start + number - first_state + REACH
        mixing = mixing + jnp.where(
            slots[None, :] == target[:, None], (earn_prob[number] / prob_sum)[:, None], 0.0
        )
    return jnp.einsum("ij,tjxy->tixy", mixing, padded, precision=lax.Precision.HIGH)


def along_lanes(stacked, matrix):
    return jnp.einsum("terc,ecn->tern", stacked, matrix, precision=lax.Precision.HIGH)


def _gather_kernel(src_ref, dst_ref):
    count, piece, lanes = src_ref.shape
    width = dst_ref.shape[2] // count
    slabs = 128 // width
    lane = lax.broadcasted_iota(jnp.int32, (piece, 128), 1)
    for k in range(lanes // 128):
        for w in range(count // slabs):
            outs = [None] * slabs
            for u in range(slabs):
                x = src_ref[w * slabs + u, :, pl.ds(k * 128, 128)]
                keep = (lane >= u * width) & (lane < (u + 1) * width)
                for s in range(slabs):
                    shift = ((u - s) * width) % 128
                    y = pltpu.roll(x, shift, 1) if shift else x
                    outs[s] = y if u == 0 else jnp.where(keep, y, outs[s])
            for s in range(slabs):
                dst_ref[k * slabs + s, :, pl.ds(w * 128, 128)] = outs[s]


def regroup(got):
    count, piece, lanes = got.shape
    width = lanes // count
    nbytes = got.size * got.dtype.itemsize
    return pl.pallas_call(
        _gather_kernel,
        in_specs=[pl.BlockSpec(memory_space=pltpu.VMEM)],
        out_specs=pl.BlockSpec(memory_space=pltpu.VMEM),
        out_shape=jax.ShapeDtypeStruct((lanes // width, piece, count * width), got.dtype),
        cost_estimate=pl.CostEstimate(flops=0, transcendentals=0, bytes_accessed=2 * nbytes),
    )(got)


def flipped(stacked):
    ages, states, rows, lanes = stacked.shape
    count = lax.axis_size("asset")
    piece = lanes // count
    flat = stacked.reshape(ages * states * rows, lanes).T.reshape(count, piece, ages * states * rows)
    got = lax.all_to_all(flat, "asset", 0, 0, tiled=True)
    return regroup(got).reshape(ages, states, piece, count * rows)


def local(
    values,
    utility,
    earn_prob,
    support_start,
    liquid_offset,
    liquid_weight,
    illiquid_offset,
    illiquid_weight,
):
    liquid_map = lax.optimization_barrier(band_matrix(liquid_offset, liquid_weight))
    here, above = neighbours(values)
    first = mix(here, earn_prob, support_start)
    first, utility_sent = lax.optimization_barrier((first, utility))
    saved = jnp.concatenate(
        [along_lanes(first, liquid_map), along_lanes(mix(above, earn_prob, support_start), liquid_map)], axis=0
    )
    saved, illiquid_offset, illiquid_weight = lax.optimization_barrier(
        (saved, illiquid_offset, illiquid_weight)
    )
    illiquid_map = lax.optimization_barrier(band_matrix(illiquid_offset, illiquid_weight))
    adjusted = along_lanes(flipped(saved), illiquid_map)
    current = flipped(utility_sent) + DISCOUNT * adjusted

    expected = continuation(current, earn_prob, support_start)
    moved = along_lanes(expected, illiquid_map)
    adjusted = along_lanes(flipped(moved), liquid_map)
    return utility + DISCOUNT * adjusted


def solution(mesh):
    return jax.shard_map(
        local,
        mesh=mesh,
        in_specs=(
            P("age", "earn", "asset", None),
            P("age", "earn", "asset", None),
            P(None, "earn"),
            P("earn"),
            P("earn", None),
            P(None, "earn", None),
            P("earn", None),
            P(None, "earn", None),
        ),
        out_specs=P("age", "earn", "asset", None),
        check_vma=False,
    )
```

```python
import jax
import jax.numpy as jnp
from jax import lax
from jax.experimental import pallas as pl
from jax.experimental.pallas import tpu as pltpu
from jax.sharding import PartitionSpec as P

REACH = 4
BAND = 4
ITERS = 2


DISCOUNT = 0.96
PRECISE = lax.Precision.HIGHEST


def band_matrix(offset, weight):
    extent = offset.shape[1]
    positions = jnp.arange(extent, dtype=jnp.int32)
    matrix = jnp.zeros((offset.shape[0], extent, extent), jnp.float32)
    for number in range(BAND):
        matrix = matrix + jnp.where(
            positions[None, :, None] == (offset + number)[:, None, :],
            weight[number][:, None, :],
            0.0,
        )
    return matrix


def neighbours(current):
    states = current.shape[1]
    ages = lax.axis_size("age")
    earns = lax.axis_size("earn")
    axes = ("earn", "age")

    def moved(value, by_earn, by_age):
        pairs = []
        for e in range(earns):
            for a in range(ages):
                te, ta = e + by_earn, a + by_age
                if 0 <= te < earns and 0 <= ta < ages:
                    pairs.append((e * ages + a, te * ages + ta))
        return lax.ppermute(value, axes, pairs)

    head = slice(0, REACH)
    tail = slice(states - REACH, states)
    here = jnp.concatenate(
        [moved(current[1:, tail], 1, 0), current[1:], moved(current[1:, head], -1, 0)], axis=1
    )
    above = jnp.concatenate(
        [moved(current[:1, tail], 1, -1), moved(current[:1], 0, -1), moved(current[:1, head], -1, -1)],
        axis=1,
    )
    return here, above


def continuation(current, earn_prob, support_start):
    return jnp.concatenate([mix(part, earn_prob, support_start) for part in neighbours(current)], axis=0)


def mix(padded, earn_prob, support_start):
    states_here = padded.shape[1] - 2 * REACH
    first_state = lax.axis_index("earn") * states_here
    slots = jnp.arange(states_here + 2 * REACH, dtype=jnp.int32)
    prob_sum = jnp.sum(earn_prob, axis=0)
    mixing = jnp.zeros((states_here, states_here + 2 * REACH), jnp.float32)
    for number in range(REACH + 1):
        target = support_start + number - first_state + REACH
        mixing = mixing + jnp.where(
            slots[None, :] == target[:, None], (earn_prob[number] / prob_sum)[:, None], 0.0
        )
    return jnp.einsum("ij,tjxy->tixy", mixing, padded, precision=lax.Precision.HIGH)


def along_lanes(stacked, matrix):
    return jnp.einsum("terc,ecn->tern", stacked, matrix, precision=lax.Precision.HIGH)


def _gather_kernel(src_ref, dst_ref):
    count, piece, lanes = src_ref.shape
    width = dst_ref.shape[2] // count
    slabs = 128 // width
    lane = lax.broadcasted_iota(jnp.int32, (piece, 128), 1)
    for k in range(lanes // 128):
        for w in range(count // slabs):
            outs = [None] * slabs
            for u in range(slabs):
                x = src_ref[w * slabs + u, :, pl.ds(k * 128, 128)]
                keep = (lane >= u * width) & (lane < (u + 1) * width)
                for s in range(slabs):
                    shift = ((u - s) * width) % 128
                    y = pltpu.roll(x, shift, 1) if shift else x
                    outs[s] = y if u == 0 else jnp.where(keep, y, outs[s])
            for s in range(slabs):
                dst_ref[k * slabs + s, :, pl.ds(w * 128, 128)] = outs[s]


def regroup(got):
    count, piece, lanes = got.shape
    width = lanes // count
    nbytes = got.size * got.dtype.itemsize
    return pl.pallas_call(
        _gather_kernel,
        in_specs=[pl.BlockSpec(memory_space=pltpu.VMEM)],
        out_specs=pl.BlockSpec(memory_space=pltpu.VMEM),
        out_shape=jax.ShapeDtypeStruct((lanes // width, piece, count * width), got.dtype),
        cost_estimate=pl.CostEstimate(flops=0, transcendentals=0, bytes_accessed=2 * nbytes),
    )(got)


def flipped(stacked):
    ages, states, rows, lanes = stacked.shape
    count = lax.axis_size("asset")
    piece = lanes // count
    flat = stacked.reshape(ages * states * rows, lanes).T.reshape(count, piece, ages * states * rows)
    got = lax.all_to_all(flat, "asset", 0, 0, tiled=True)
    return regroup(got).reshape(ages, states, piece, count * rows)


def local(
    values,
    utility,
    earn_prob,
    support_start,
    liquid_offset,
    liquid_weight,
    illiquid_offset,
    illiquid_weight,
):
    liquid_map = lax.optimization_barrier(band_matrix(liquid_offset, liquid_weight))
    saved = jnp.concatenate(
        [along_lanes(mix(part, earn_prob, support_start), liquid_map) for part in neighbours(values)], axis=0
    )
    saved, illiquid_offset, illiquid_weight = lax.optimization_barrier(
        (saved, illiquid_offset, illiquid_weight)
    )
    illiquid_map = lax.optimization_barrier(band_matrix(illiquid_offset, illiquid_weight))
    arrived = flipped(saved)
    carried = flipped(utility)
    current = jnp.concatenate(
        [carried[t : t + 1] + DISCOUNT * along_lanes(arrived[t : t + 1], illiquid_map) for t in range(2)], axis=0
    )

    expected = continuation(current, earn_prob, support_start)
    moved = along_lanes(expected, illiquid_map)
    adjusted = along_lanes(flipped(moved), liquid_map)
    return utility + DISCOUNT * adjusted


def solution(mesh):
    return jax.shard_map(
        local,
        mesh=mesh,
        in_specs=(
            P("age", "earn", "asset", None),
            P("age", "earn", "asset", None),
            P(None, "earn"),
            P("earn"),
            P("earn", None),
            P(None, "earn", None),
            P("earn", None),
            P(None, "earn", None),
        ),
        out_specs=P("age", "earn", "asset", None),
        check_vma=False,
    )
```
